512 devices in a mesh: section: 16 (over y, core), expert: 32 (over z, x).
Axes of the slice: x: 4, y: 8, z: 8, core: 2. Of those that a mesh axis runs over, the one named last changes fastest.
Arguments:
- acts: bfloat16 [16, 4, 1024, 1024], P('section', None, 'expert'), may hold values from -6 to 6
- carried: bfloat16 [16, 1024, 1024], P('section', 'expert'), may hold values from -6 to 6
- loss_grad: bfloat16 [4, 1024, 1024], P(None, 'expert'), may hold values from -6 to 6
- expert_ids: int32 [16, 4, 1024, 8], P('section', None, 'expert'), may hold values from 0 to 31, all different within a row; in each aligned block of 32 rows (0 to 31, 32 to 63, ..., all dimensions but the last counted through in order) at most 12 rows name the same one
- probs: float32 [16, 4, 1024, 8], P('section', None, 'expert'), may hold values from 0.1 to 0.4
- w_gate: bfloat16 [16, 32, 1024, 384], P('section', 'expert'), may hold values from -0.1875 to 0.1875
- w_up: bfloat16 [16, 32, 1024, 384], P('section', 'expert'), may hold values from -0.1875 to 0.1875
- w_down: bfloat16 [16, 32, 384, 1024], P('section', 'expert'), may hold values from -0.3125 to 0.3125
Outputs:
- out_grad: bfloat16 [16, 4, 1024, 1024], P('section', None, 'expert')
- down_grad: bfloat16 [16, 32, 384, 1024], P('section', 'expert')
The draws below stay inside these ranges and needn't reach their ends.
Inputs may be any that keep to these rules, and one draw needn't show every extreme that they name: `expert_ids`: in each aligned block of 32 tokens of one section and tick, no expert is named by more than 12 of the block's pairs, and in every draw some block has an expert named by exactly 12.
All inputs are finite; a program needn't handle non-finite values.
Results may differ from the reference program's by a relative error of at most 0.0095.
Values may be sent and summed in bfloat16 or wider, within the bound.
No kernel may reach another device: no remote copies, remote signals or barrier semaphores. Data moves between devices by JAX's collectives and lax.ppermute only.
A program may use at most 64 MiB of HBM per device.

```python
import math
import jax
import jax.numpy as jnp
import numpy as np
from jax import lax

D = 1024
FF = 384
TOPK = 8
TICKS = 4
TOK = 32
SECTIONS = 16
EXPERTS = 32
TOKENS = 1024
SLOT = 12


def levels(rng, shape, shards, low, top_value):
    def one(dim, shards_of):
        steps = jax.random.uniform(jax.random.fold_in(jax.random.fold_in(rng, 6), dim), (shards_of,), jnp.float32, low / len(shards), top_value / len(shards))
        return jnp.repeat(jnp.exp(steps), shape[dim] // shards_of).reshape((-1,) + (1,) * (len(shape) - dim - 1))

    gain = one(*shards[0])
    for cut in shards[1:]:
        gain = gain * one(*cut)
    return gain


def deal_out(rng, own, number, rows, amount, top, bound, lean):
    ranking = jax.random.permutation(rng, amount)
    heavy_load, usual = shares(amount, rows * top, bound, lean, True), shares(amount, rows * top, bound, lean, False)
    places = jnp.arange(amount)

    def named(sizes, offset_by):
        used = int((sizes > 0).sum())
        fixed = max(1, used // 4)
        shifted = fixed + (places - fixed + offset_by * (used - fixed)) % max(1, amount - fixed)
        return jnp.zeros((amount,), jnp.int32).at[ranking[jnp.where(places < fixed, places, shifted)]].set(jnp.asarray(sizes, jnp.int32))

    sizes = jnp.where(number % 4 == 0, named(heavy_load, number // 4), named(usual, number - number // 4 - 1))
    mixed = jax.random.permutation(jax.random.fold_in(own, 3), amount)
    giver, receiver = mixed[0:amount // 2 * 2:2], mixed[1:amount // 2 * 2:2]
    slack = jnp.minimum(sizes[giver] - 1, bound - sizes[receiver]) // 2
    slack = jnp.where((giver == ranking[0]) | (receiver == ranking[0]) | (sizes[receiver] == 0), 0, jnp.maximum(slack, 0))
    shifted = jax.random.randint(jax.random.fold_in(own, 4), (amount // 2,), 0, 1 << 20) % (slack + 1)
    sizes = sizes.at[giver].add(-shifted).at[receiver].add(shifted)
    members = jnp.searchsorted(jnp.cumsum(sizes), jnp.arange(rows * top), side="right").astype(jnp.int32)
    listing = members.reshape(top, rows).T
    listing = listing[jax.random.permutation(jax.random.fold_in(own, 1), rows)]
    offset_by = jax.random.randint(jax.random.fold_in(own, 2), (rows, 1), 0, top)
    return jnp.take_along_axis(listing, (jnp.arange(top)[None, :] + offset_by) % top, axis=1)


def shares(count, total, reach, lean, full):
    loads = [(1 << 20) // math.isqrt(grade ** lean) + 1 for grade in range(1, count + 1)]
    largest = reach if full else min(reach, max(-(-total // count), total * loads[0] // sum(loads)))
    least = 1 if total - largest >= count - 1 else 0
    given, spare = [largest] + [least] * (count - 1), total - largest - least * (count - 1)
    while spare > 0:
        movable = [i for i in range(1, count) if given[i] < largest] or [i for i in range(1, count) if given[i] < reach]
        pool, left = sum([loads[i] for i in movable]), spare
        for i in movable:
            more = min(reach - given[i], max(1, left * loads[i] // pool), spare)
            given[i] = given[i] + more
            spare = spare - more
    return np.array(given)


def bell_draw(own_key, dims, spread, bound, split=(), held_as=jnp.bfloat16):
    factor_of = levels(own_key, dims, split, -0.22, 0.18) if split else 1.0
    values = jax.random.normal(own_key, dims, jnp.float32) * spread * factor_of
    return jnp.minimum(jnp.maximum(values, -bound), bound).astype(held_as)


def setup_inputs(seed: int = 0) -> dict:
    key_of = jax.random.split(jax.random.key(seed), 9)
    acts = bell_draw(key_of[0], (SECTIONS, TICKS, TOKENS, D), 1.0, 6.0, ((0, 16), (2, 32)))
    carried = bell_draw(key_of[1], (SECTIONS, TOKENS, D), 1.0, 6.0, ((0, 16), (1, 32)))
    loss_grad = bell_draw(key_of[2], (TICKS, TOKENS, D), 1.0, 6.0, ((1, 32),))
    expert_ids_keys = jax.random.split(jax.random.fold_in(key_of[3], 1), SECTIONS * TICKS * TOKENS // TOK)
    expert_ids_turns = jax.random.permutation(jax.random.fold_in(key_of[3], 3), SECTIONS * TICKS * TOKENS // TOK)
    expert_ids = jax.vmap(lambda own, number: deal_out(jax.random.fold_in(key_of[3], 2), own, number, TOK, EXPERTS, TOPK, SLOT, 2))(expert_ids_keys, expert_ids_turns).reshape((SECTIONS, TICKS, TOKENS, TOPK))
    probs = jnp.clip(0.1 + 0.3 * jax.random.uniform(key_of[4], (SECTIONS, TICKS, TOKENS, TOPK), jnp.float32) ** levels(key_of[4], (SECTIONS, TICKS, TOKENS, TOPK), ((0, 16), (2, 32)), -0.2, 0.2), 0.1, 0.4)
    w_gate = bell_draw(key_of[5], (SECTIONS, EXPERTS, D, FF), D ** -0.5, 0.1875, ((0, 16), (1, 32)))
    w_up = bell_draw(key_of[6], (SECTIONS, EXPERTS, D, FF), D ** -0.5, 0.1875, ((0, 16), (1, 32)))
    w_down = bell_draw(key_of[7], (SECTIONS, EXPERTS, FF, D), FF ** -0.5, 0.3125, ((0, 16), (1, 32)))
    return dict(acts=acts, carried=carried, loss_grad=loss_grad, expert_ids=expert_ids, probs=probs, w_gate=w_gate, w_up=w_up, w_down=w_down)


def slot_layout(expert_ids):
    tokens_all = expert_ids.shape[0]
    sources = tokens_all // TOK
    onehot = (expert_ids[:, :, None] == jnp.arange(EXPERTS, dtype=jnp.int32)[None, None, :]).astype(jnp.int32)
    blocks = onehot.reshape(sources, TOK * TOPK, EXPERTS)
    before = (jnp.cumsum(blocks, axis=1) - blocks).astype(jnp.int32)
    position = jnp.sum(before * blocks, axis=2).astype(jnp.int32).reshape(tokens_all, TOPK)
    source = (jnp.arange(tokens_all, dtype=jnp.int32) // TOK)[:, None]
    return (expert_ids * (sources * SLOT) + source * SLOT + position).astype(jnp.int32)


def backward_step(acts, grad_in, expert_ids, probs, w_gate, w_up, w_down):
    tokens_all = acts.shape[0]
    sources = tokens_all // TOK
    total = EXPERTS * sources * SLOT
    flat = slot_layout(expert_ids).reshape(-1)
    token_of_pair = jnp.repeat(jnp.arange(tokens_all, dtype=jnp.int32), TOPK)
    owner = jnp.full((total,), tokens_all, jnp.int32).at[flat].set(token_of_pair)
    weight = jnp.zeros((total,), jnp.float32).at[flat].set(probs.reshape(-1).astype(jnp.float32))
    padded_acts = jnp.concatenate([acts, jnp.zeros((1, D), acts.dtype)], 0)
    padded_grad = jnp.concatenate([grad_in, jnp.zeros((1, D), grad_in.dtype)], 0)
    input_rows = padded_acts[owner].reshape(EXPERTS, sources * SLOT, D)
    grad_rows = (padded_grad[owner].astype(jnp.float32) * weight[:, None]).astype(jnp.bfloat16)
    grad_rows = grad_rows.reshape(EXPERTS, sources * SLOT, D)
    rows_wide = input_rows.astype(jnp.float32)
    gate_wide = w_gate.astype(jnp.float32)
    up_wide = w_up.astype(jnp.float32)
    gate_pre = jnp.einsum("erd,edf->erf", rows_wide, gate_wide)
    up_pre = jnp.einsum("erd,edf->erf", rows_wide, up_wide)
    sigma = jax.nn.sigmoid(gate_pre)
    active = gate_pre * sigma
    hidden = (active * up_pre).astype(jnp.bfloat16)
    grads_wide = grad_rows.astype(jnp.float32)
    hidden_grad = jnp.einsum("erd,efd->erf", grads_wide, w_down.astype(jnp.float32))
    gate_grad = (hidden_grad * up_pre * sigma * (1.0 + gate_pre * (1.0 - sigma))).astype(jnp.bfloat16)
    up_grad = (hidden_grad * active).astype(jnp.bfloat16)
    row_grad = jnp.einsum("erf,edf->erd", gate_grad.astype(jnp.float32), gate_wide)
    row_grad = row_grad + jnp.einsum("erf,edf->erd", up_grad.astype(jnp.float32), up_wide)
    row_grad = row_grad.astype(jnp.bfloat16)
    down_term = jnp.einsum("erf,erd->efd", hidden.astype(jnp.float32), grads_wide)
    gathered = row_grad.reshape(total, D)[flat].reshape(tokens_all, TOPK, D).astype(jnp.float32)
    result = (grad_in.astype(jnp.float32) + jnp.sum(gathered, axis=1)).astype(jnp.bfloat16)
    return result, down_term


def section_pass(incoming, acts, expert_ids, probs, w_gate, w_up, w_down):
    results = []
    down_sum = jnp.zeros((EXPERTS, FF, D), jnp.float32)
    for moment in range(TICKS):
        result, term = backward_step(acts[moment], incoming[moment], expert_ids[moment], probs[moment], w_gate, w_up, w_down)
        results.append(result)
        down_sum = down_sum + term
    return jnp.stack(results, axis=0), down_sum.astype(jnp.bfloat16)


def reference(acts, carried, loss_grad, expert_ids, probs, w_gate, w_up, w_down):
    last = acts.shape[0] - 1
    top_out, top_down = section_pass(loss_grad, acts[last], expert_ids[last], probs[last], w_gate[last], w_up[last], w_down[last])

    def step_down(above, pieces):
        carried_one, acts_one, ids_one, probs_one, gate_one, up_one, down_one = pieces
        incoming = jnp.concatenate([carried_one[None], above[:-1]], 0)
        result, down_one_grad = section_pass(incoming, acts_one, ids_one, probs_one, gate_one, up_one, down_one)
        return result, (result, down_one_grad)

    unused, stacked = lax.scan(step_down, top_out, (carried[:-1], acts[:-1], expert_ids[:-1], probs[:-1], w_gate[:-1], w_up[:-1], w_down[:-1]), reverse=True)
    rest_out, rest_down = stacked
    out_grad = jnp.concatenate([rest_out, top_out[None]], 0)
    down_grad = jnp.concatenate([rest_down, top_down[None]], 0)
    return out_grad, down_grad
```

```python
import jax
import jax.numpy as jnp
from jax import lax
from jax.sharding import PartitionSpec as P

TOPK = 8
LANES = 128


def passed_along(value, axis, steps):
    count = lax.axis_size(axis)
    leading, last = (max(0, -steps), min(count, count - steps))
    return lax.ppermute(value, axis, [(source, source + steps) for source in range(leading, last)])


def slot_tables(expert_ids, probs, experts, slot_rows):
    tokens_here, choices_here = expert_ids.shape
    onehot = (expert_ids[:, :, None] == jnp.arange(experts, dtype=jnp.int32)[None, None, :]).astype(
        jnp.int32
    )
    pairs = onehot.reshape(tokens_here * choices_here, experts)
    before = jnp.cumsum(pairs, axis=0) - pairs
    position = jnp.sum(before * pairs, axis=1).reshape(tokens_here, choices_here)
    target = expert_ids * slot_rows + position
    match = target[None, :, :] == jnp.arange(experts * slot_rows, dtype=jnp.int32)[:, None, None]
    select = jnp.any(match, axis=2).astype(jnp.bfloat16)
    weight = jnp.sum(jnp.where(match, probs[None, :, :], 0.0), axis=(1, 2))
    return (select, weight)


def select_rows(select, source):
    return jnp.dot(select, source, preferred_element_type=jnp.float32)


def pack(rows, experts):
    return rows.reshape(experts, -1, LANES)


def unpack(block, width):
    return block.reshape(-1, width)


def exchange(block):
    return lax.all_to_all(block, "expert", split_axis=0, concat_axis=0, tiled=True)


def expert_backward(gate_pre, up_pre, sigma, grad_rows, gate_weight, up_weight, down_weight):
    contract = (((1,), (1,)), ((), ()))
    active = gate_pre * sigma
    hidden_grad = lax.dot_general(
        grad_rows, down_weight, contract, preferred_element_type=jnp.float32
    )
    gate_grad = (hidden_grad * up_pre * sigma * (1.0 + gate_pre * (1.0 - sigma))).astype(
        jnp.bfloat16
    )
    up_grad = (hidden_grad * active).astype(jnp.bfloat16)
    row_grad = lax.dot_general(gate_grad, gate_weight, contract, preferred_element_type=jnp.float32)
    row_grad = row_grad + lax.dot_general(
        up_grad, up_weight, contract, preferred_element_type=jnp.float32
    )
    return row_grad.astype(jnp.bfloat16)


def per_device(acts, carried, loss_grad, expert_ids, probs, w_gate, w_up, w_down):
    experts = lax.axis_size("expert")
    ticks_here = acts.shape[1]
    tokens_here = acts.shape[2]
    width = acts.shape[3]
    slot_rows = min(tokens_here, 3 * tokens_here * TOPK // (2 * experts))
    rows_here = experts * slot_rows
    gate_weight = w_gate[0, 0]
    up_weight = w_up[0, 0]
    down_weight = w_down[0, 0]
    is_last = lax.axis_index("section") == lax.axis_size("section") - 1
    tables = [
        slot_tables(expert_ids[0, moment], probs[0, moment], experts, slot_rows)
        for moment in range(ticks_here)
    ]
    rows_contract = (((0,), (0,)), ((), ()))

    def grad_rows_of(moment, incoming):
        select, weight = tables[moment]
        return (select_rows(select, incoming) * weight[:, None]).astype(jnp.bfloat16)

    incoming = jnp.where(is_last, loss_grad[0], carried[0])
    parts = [
        select_rows(tables[moment][0], acts[0, moment]).astype(jnp.bfloat16)
        for moment in range(ticks_here)
    ]
    parts.append(grad_rows_of(0, incoming))
    send = jnp.stack([pack(part, experts) for part in parts], axis=1)
    count = len(parts)
    received = exchange(send.reshape(experts, -1, LANES)).reshape(experts, count, -1, LANES)
    received_inputs = jnp.concatenate(
        [unpack(received[:, moment], width) for moment in range(ticks_here)], axis=0
    )
    flat_grad = unpack(received[:, ticks_here], width)

    gate_all = jnp.dot(received_inputs, gate_weight, preferred_element_type=jnp.float32)
    up_all = jnp.dot(received_inputs, up_weight, preferred_element_type=jnp.float32)
    sigma_all = jax.nn.sigmoid(gate_all)
    hidden_all = (gate_all * sigma_all * up_all).astype(jnp.bfloat16)

    results = []
    down_sum = jnp.zeros((down_weight.shape[0], width), jnp.float32)
    for moment in range(ticks_here):
        rows = slice(moment * rows_here, (moment + 1) * rows_here)
        row_grad = expert_backward(
            gate_all[rows], up_all[rows], sigma_all[rows], flat_grad, gate_weight, up_weight,
            down_weight,
        )
        returned = unpack(exchange(pack(row_grad, experts)), width)
        gathered = lax.dot_general(
            tables[moment][0], returned, rows_contract, preferred_element_type=jnp.float32
        )
        result = (incoming.astype(jnp.float32) + gathered).astype(jnp.bfloat16)
        results.append(result)
        down_sum = down_sum + lax.dot_general(
            hidden_all[rows], flat_grad, rows_contract, preferred_element_type=jnp.float32
        )
        if moment + 1 < ticks_here:
            arriving = passed_along(result, "section", -1)
            incoming = jnp.where(is_last, loss_grad[moment + 1], arriving)
            flat_grad = unpack(exchange(pack(grad_rows_of(moment + 1, incoming), experts)), width)
    out_grad = jnp.stack(results, axis=0)[None]
    return (out_grad, down_sum.astype(jnp.bfloat16)[None, None])


def solution(mesh):
    return jax.shard_map(
        per_device,
        mesh=mesh,
        in_specs=(
            P("section", None, "expert", None),
            P("section", "expert", None),
            P(None, "expert", None),
            P("section", None, "expert", None),
            P("section", None, "expert", None),
            P("section", "expert", None, None),
            P("section", "expert", None, None),
            P("section", "expert", None, None),
        ),
        out_specs=(P("section", None, "expert", None), P("section", "expert", None, None)),
        check_vma=False,
    )
```

```python
import jax
import jax.numpy as jnp
from jax import lax
from jax.sharding import PartitionSpec as P

TOPK = 8
LANES = 128


def passed_along(value, axis, steps):
    count = lax.axis_size(axis)
    leading, last = (max(0, -steps), min(count, count - steps))
    return lax.ppermute(value, axis, [(source, source + steps) for source in range(leading, last)])


def slot_tables(expert_ids, probs, experts, slot_rows):
    tokens_here, choices_here = expert_ids.shape
    onehot = (expert_ids[:, :, None] == jnp.arange(experts, dtype=jnp.int32)[None, None, :]).astype(
        jnp.int32
    )
    pairs = onehot.reshape(tokens_here * choices_here, experts)
    before = jnp.cumsum(pairs, axis=0) - pairs
    position = jnp.sum(before * pairs, axis=1).reshape(tokens_here, choices_here)
    target = expert_ids * slot_rows + position
    match = target[None, :, :] == jnp.arange(experts * slot_rows, dtype=jnp.int32)[:, None, None]
    select = jnp.any(match, axis=2).astype(jnp.bfloat16)
    weight = jnp.sum(jnp.where(match, probs[None, :, :], 0.0), axis=(1, 2))
    return (select, weight)


def select_rows(select, source):
    return jnp.dot(select, source, preferred_element_type=jnp.float32)


def pack(rows, experts):
    return rows.reshape(experts, -1, LANES)


def unpack(block, width):
    return block.reshape(-1, width)


def exchange(block):
    return lax.all_to_all(block, "expert", split_axis=0, concat_axis=0, tiled=True)


def expert_backward(gate_pre, up_pre, sigma, grad_rows, gate_weight, up_weight, down_weight):
    contract = (((1,), (1,)), ((), ()))
    active = gate_pre * sigma
    hidden_grad = lax.dot_general(
        grad_rows, down_weight, contract, preferred_element_type=jnp.float32
    )
    gate_grad = (hidden_grad * up_pre * sigma * (1.0 + gate_pre * (1.0 - sigma))).astype(
        jnp.bfloat16
    )
    up_grad = (hidden_grad * active).astype(jnp.bfloat16)
    row_grad = lax.dot_general(gate_grad, gate_weight, contract, preferred_element_type=jnp.float32)
    row_grad = row_grad + lax.dot_general(
        up_grad, up_weight, contract, preferred_element_type=jnp.float32
    )
    return row_grad.astype(jnp.bfloat16)


def expert_tables(ids_all, probs_all, expert, blocks, slot_rows):
    hit = ids_all == expert
    present = jnp.any(hit, axis=1)
    chance = jnp.sum(jnp.where(hit, probs_all, 0.0), axis=1)
    mark = present.astype(jnp.int32).reshape(blocks, -1)
    position = (jnp.cumsum(mark, axis=1) - mark).reshape(-1)
    block_of = jnp.arange(ids_all.shape[0], dtype=jnp.int32) // mark.shape[1]
    target = jnp.where(present, block_of * slot_rows + position, -1)
    match = target[None, :] == jnp.arange(blocks * slot_rows, dtype=jnp.int32)[:, None]
    select = match.astype(jnp.bfloat16)
    weight = jnp.sum(jnp.where(match, chance[None, :], 0.0), axis=1)
    return (select, weight)


def per_device(acts, carried, loss_grad, expert_ids, probs, w_gate, w_up, w_down):
    experts = lax.axis_size("expert")
    expert = lax.axis_index("expert")
    ticks_here = acts.shape[1]
    tokens_here = acts.shape[2]
    width = acts.shape[3]
    slot_rows = min(tokens_here, 3 * tokens_here * TOPK // (2 * experts))
    gate_weight = w_gate[0, 0]
    up_weight = w_up[0, 0]
    down_weight = w_down[0, 0]
    is_last = lax.axis_index("section") == lax.axis_size("section") - 1
    tables = [
        slot_tables(expert_ids[0, moment], probs[0, moment], experts, slot_rows)
        for moment in range(ticks_here)
    ]
    rows_contract = (((0,), (0,)), ((), ()))

    def grad_rows_of(moment, incoming):
        select, weight = tables[moment]
        return (select_rows(select, incoming) * weight[:, None]).astype(jnp.bfloat16)

    incoming = jnp.where(is_last, loss_grad[0], carried[0])
    ids_all = lax.all_gather(expert_ids[0], "expert", axis=1, tiled=True)
    probs_all = lax.all_gather(probs[0], "expert", axis=1, tiled=True)
    incoming_all = lax.all_gather(incoming, "expert", axis=0, tiled=True)
    own = [
        expert_tables(ids_all[moment], probs_all[moment], expert, experts, slot_rows)
        for moment in range(ticks_here)
    ]
    input_parts = []
    for moment in range(ticks_here):
        acts_all = lax.all_gather(acts[0, moment], "expert", axis=0, tiled=True)
        input_parts.append(select_rows(own[moment][0], acts_all).astype(jnp.bfloat16))
    flat_grad = (select_rows(own[0][0], incoming_all) * own[0][1][:, None]).astype(jnp.bfloat16)

    results = []
    down_sum = jnp.zeros((down_weight.shape[0], width), jnp.float32)
    for moment in range(ticks_here):
        gate_pre = jnp.dot(input_parts[moment], gate_weight, preferred_element_type=jnp.float32)
        up_pre = jnp.dot(input_parts[moment], up_weight, preferred_element_type=jnp.float32)
        sigma = jax.nn.sigmoid(gate_pre)
        hidden = (gate_pre * sigma * up_pre).astype(jnp.bfloat16)
        row_grad = expert_backward(
            gate_pre, up_pre, sigma, flat_grad, gate_weight, up_weight, down_weight
        )
        returned = unpack(exchange(pack(row_grad, experts)), width)
        gathered = lax.dot_general(
            tables[moment][0], returned, rows_contract, preferred_element_type=jnp.float32
        )
        result = (incoming.astype(jnp.float32) + gathered).astype(jnp.bfloat16)
        results.append(result)
        down_sum = down_sum + lax.dot_general(
            hidden, flat_grad, rows_contract, preferred_element_type=jnp.float32
        )
        if moment + 1 < ticks_here:
            arriving = passed_along(result, "section", -1)
            incoming = jnp.where(is_last, loss_grad[moment + 1], arriving)
            flat_grad = unpack(exchange(pack(grad_rows_of(moment + 1, incoming), experts)), width)
    out_grad = jnp.stack(results, axis=0)[None]
    return (out_grad, down_sum.astype(jnp.bfloat16)[None, None])


def solution(mesh):
    return jax.shard_map(
        per_device,
        mesh=mesh,
        in_specs=(
            P("section", None, "expert", None),
            P("section", "expert", None),
            P(None, "expert", None),
            P("section", None, "expert", None),
            P("section", None, "expert", None),
            P("section", "expert", None, None),
            P("section", "expert", None, None),
            P("section", "expert", None, None),
        ),
        out_specs=(P("section", None, "expert", None), P("section", "expert", None, None)),
        check_vma=False,
    )
```

```python
import jax
import jax.numpy as jnp
from jax import lax
from jax.sharding import PartitionSpec as P

TOPK = 8
LANES = 128


def passed_along(value, axis, steps):
    count = lax.axis_size(axis)
    leading, last = (max(0, -steps), min(count, count - steps))
    return lax.ppermute(value, axis, [(source, source + steps) for source in range(leading, last)])


def slot_tables(expert_ids, probs, experts, slot_rows):
    tokens_here, choices_here = expert_ids.shape
    onehot = (expert_ids[:, :, None] == jnp.arange(experts, dtype=jnp.int32)[None, None, :]).astype(
        jnp.int32
    )
    pairs = onehot.reshape(tokens_here * choices_here, experts)
    before = jnp.cumsum(pairs, axis=0) - pairs
    position = jnp.sum(before * pairs, axis=1).reshape(tokens_here, choices_here)
    target = expert_ids * slot_rows + position
    match = target[None, :, :] == jnp.arange(experts * slot_rows, dtype=jnp.int32)[:, None, None]
    select = jnp.any(match, axis=2).astype(jnp.bfloat16)
    weight = jnp.sum(jnp.where(match, probs[None, :, :], 0.0), axis=(1, 2))
    return (select, weight)


def select_rows(select, source):
    return jnp.dot(select, source, preferred_element_type=jnp.float32)


def pack(rows, experts):
    return rows.reshape(experts, -1, LANES)


def unpack(block, width):
    return block.reshape(-1, width)


def exchange(block):
    return lax.all_to_all(block, "expert", split_axis=0, concat_axis=0, tiled=True)


def expert_backward(gate_pre, up_pre, sigma, grad_rows, gate_weight, up_weight, down_weight):
    contract = (((1,), (1,)), ((), ()))
    active = gate_pre * sigma
    hidden_grad = lax.dot_general(
        grad_rows, down_weight, contract, preferred_element_type=jnp.float32
    )
    gate_grad = (hidden_grad * up_pre * sigma * (1.0 + gate_pre * (1.0 - sigma))).astype(
        jnp.bfloat16
    )
    up_grad = (hidden_grad * active).astype(jnp.bfloat16)
    row_grad = lax.dot_general(gate_grad, gate_weight, contract, preferred_element_type=jnp.float32)
    row_grad = row_grad + lax.dot_general(
        up_grad, up_weight, contract, preferred_element_type=jnp.float32
    )
    return row_grad.astype(jnp.bfloat16)


def per_device(acts, carried, loss_grad, expert_ids, probs, w_gate, w_up, w_down):
    experts = lax.axis_size("expert")
    ticks_here = acts.shape[1]
    tokens_here = acts.shape[2]
    width = acts.shape[3]
    slot_rows = min(tokens_here, 3 * tokens_here * TOPK // (2 * experts))
    gate_weight = w_gate[0, 0]
    up_weight = w_up[0, 0]
    down_weight = w_down[0, 0]
    is_last = lax.axis_index("section") == lax.axis_size("section") - 1
    tables = [
        slot_tables(expert_ids[0, moment], probs[0, moment], experts, slot_rows)
        for moment in range(ticks_here)
    ]
    rows_contract = (((0,), (0,)), ((), ()))

    def grad_rows_of(moment, incoming):
        select, weight = tables[moment]
        return (select_rows(select, incoming) * weight[:, None]).astype(jnp.bfloat16)

    incoming = jnp.where(is_last, loss_grad[0], carried[0])
    parts = [
        select_rows(tables[moment][0], acts[0, moment]).astype(jnp.bfloat16)
        for moment in range(ticks_here)
    ]
    parts.append(grad_rows_of(0, incoming))
    send = jnp.stack([pack(part, experts) for part in parts], axis=1)
    count = len(parts)
    received = exchange(send.reshape(experts, -1, LANES)).reshape(experts, count, -1, LANES)
    flat_grad = unpack(received[:, ticks_here], width)

    results = []
    down_sum = jnp.zeros((down_weight.shape[0], width), jnp.float32)
    for moment in range(ticks_here):
        received_input = unpack(received[:, moment], width)
        gate_pre = jnp.dot(received_input, gate_weight, preferred_element_type=jnp.float32)
        up_pre = jnp.dot(received_input, up_weight, preferred_element_type=jnp.float32)
        sigma = jax.nn.sigmoid(gate_pre)
        hidden = (gate_pre * sigma * up_pre).astype(jnp.bfloat16)
        row_grad = expert_backward(
            gate_pre, up_pre, sigma, flat_grad, gate_weight, up_weight, down_weight
        )
        returned = unpack(exchange(pack(row_grad, experts)), width)
        gathered = lax.dot_general(
            tables[moment][0], returned, rows_contract, preferred_element_type=jnp.float32
        )
        result = (incoming.astype(jnp.float32) + gathered).astype(jnp.bfloat16)
        results.append(result)
        down_sum = down_sum + lax.dot_general(
            hidden, flat_grad, rows_contract, preferred_element_type=jnp.float32
        )
        if moment + 1 < ticks_here:
            arriving = passed_along(result, "section", -1)
            incoming = jnp.where(is_last, loss_grad[moment + 1], arriving)
            flat_grad = unpack(exchange(pack(grad_rows_of(moment + 1, incoming), experts)), width)
    out_grad = jnp.stack(results, axis=0)[None]
    return (out_grad, down_sum.astype(jnp.bfloat16)[None, None])


def solution(mesh):
    return jax.shard_map(
        per_device,
        mesh=mesh,
        in_specs=(
            P("section", None, "expert", None),
            P("section", "expert", None),
            P(None, "expert", None),
            P("section", None, "expert", None),
            P("section", None, "expert", None),
            P("section", "expert", None, None),
            P("section", "expert", None, None),
            P("section", "expert", None, None),
        ),
        out_specs=(P("section", None, "expert", None), P("section", "expert", None, None)),
        check_vma=False,
    )
```

```python
import jax
import jax.numpy as jnp
from jax import lax
from jax.sharding import PartitionSpec as P

TOPK = 8
LANES = 128


def passed_along(value, axis, steps):
    count = lax.axis_size(axis)
    leading, last = (max(0, -steps), min(count, count - steps))
    return lax.ppermute(value, axis, [(source, source + steps) for source in range(leading, last)])


def slot_tables(expert_ids, probs, experts, slot_rows):
    ticks_here, tokens_here, choices_here = expert_ids.shape
    onehot = (expert_ids[..., None] == jnp.arange(experts, dtype=jnp.int32)).astype(jnp.int32)
    pairs = onehot.reshape(ticks_here, tokens_here * choices_here, experts)
    before = jnp.cumsum(pairs, axis=1) - pairs
    position = jnp.sum(before * pairs, axis=2).reshape(ticks_here, tokens_here, choices_here)
    target = expert_ids * slot_rows + position
    slots = jnp.arange(experts * slot_rows, dtype=jnp.int32)
    match = target[:, None, :, :] == slots[None, :, None, None]
    select = jnp.any(match, axis=3).astype(jnp.bfloat16)
    weight = jnp.sum(jnp.where(match, probs[:, None, :, :], 0.0), axis=(2, 3))
    return (select, weight)


def select_rows(select, source):
    return jnp.dot(select, source, preferred_element_type=jnp.float32)


def pack(rows, experts):
    return rows.reshape(experts, -1, LANES)


def unpack(block, width):
    return block.reshape(-1, width)


def exchange(block):
    return lax.all_to_all(block, "expert", split_axis=0, concat_axis=0, tiled=True)


def expert_backward(gate_pre, up_pre, sigma, grad_rows, gate_weight, up_weight, down_weight):
    contract = (((1,), (1,)), ((), ()))
    active = gate_pre * sigma
    hidden_grad = lax.dot_general(
        grad_rows, down_weight, contract, preferred_element_type=jnp.float32
    )
    gate_grad = (hidden_grad * up_pre * sigma * (1.0 + gate_pre * (1.0 - sigma))).astype(
        jnp.bfloat16
    )
    up_grad = (hidden_grad * active).astype(jnp.bfloat16)
    row_grad = lax.dot_general(gate_grad, gate_weight, contract, preferred_element_type=jnp.float32)
    row_grad = row_grad + lax.dot_general(
        up_grad, up_weight, contract, preferred_element_type=jnp.float32
    )
    return row_grad.astype(jnp.bfloat16)


def per_device(acts, carried, loss_grad, expert_ids, probs, w_gate, w_up, w_down):
    experts = lax.axis_size("expert")
    ticks_here = acts.shape[1]
    tokens_here = acts.shape[2]
    width = acts.shape[3]
    slot_rows = min(tokens_here, 3 * tokens_here * TOPK // (2 * experts))
    gate_weight = w_gate[0, 0]
    up_weight = w_up[0, 0]
    down_weight = w_down[0, 0]
    is_last = lax.axis_index("section") == lax.axis_size("section") - 1
    select_all, weight_all = slot_tables(expert_ids[0], probs[0], experts, slot_rows)
    rows_contract = (((0,), (0,)), ((), ()))

    def grad_rows_of(moment, incoming):
        select, weight = select_all[moment], weight_all[moment]
        return (select_rows(select, incoming) * weight[:, None]).astype(jnp.bfloat16)

    incoming = jnp.where(is_last, loss_grad[0], carried[0])
    count = ticks_here + 1
    chooser = jnp.concatenate([select_all, select_all[:1]], axis=0)
    sources = jnp.concatenate([acts[0], incoming[None]], axis=0)
    scale = jnp.concatenate(
        [jnp.ones((ticks_here, select_all.shape[1]), jnp.float32), weight_all[:1]], axis=0
    )
    picked = lax.dot_general(
        chooser, sources, (((2,), (1,)), ((0,), (0,))), preferred_element_type=jnp.float32
    )
    picked = (picked * scale[:, :, None]).astype(jnp.bfloat16)
    send = picked.reshape(count, experts, -1, LANES).transpose(1, 0, 2, 3)
    received = exchange(send.reshape(experts, -1, LANES)).reshape(experts, count, -1, LANES)
    flat_grad = unpack(received[:, ticks_here], width)

    results = []
    down_sum = jnp.zeros((down_weight.shape[0], width), jnp.float32)
    for moment in range(ticks_here):
        received_input = unpack(received[:, moment], width)
        gate_pre = jnp.dot(received_input, gate_weight, preferred_element_type=jnp.float32)
        up_pre = jnp.dot(received_input, up_weight, preferred_element_type=jnp.float32)
        sigma = jax.nn.sigmoid(gate_pre)
        hidden = (gate_pre * sigma * up_pre).astype(jnp.bfloat16)
        row_grad = expert_backward(
            gate_pre, up_pre, sigma, flat_grad, gate_weight, up_weight, down_weight
        )
        returned = unpack(exchange(pack(row_grad, experts)), width)
        gathered = lax.dot_general(
            select_all[moment], returned, rows_contract, preferred_element_type=jnp.float32
        )
        result = (incoming.astype(jnp.float32) + gathered).astype(jnp.bfloat16)
        results.append(result)
        down_sum = down_sum + lax.dot_general(
            hidden, flat_grad, rows_contract, preferred_element_type=jnp.float32
        )
        if moment + 1 < ticks_here:
            arriving = passed_along(result, "section", -1)
            incoming = jnp.where(is_last, loss_grad[moment + 1], arriving)
            flat_grad = unpack(exchange(pack(grad_rows_of(moment + 1, incoming), experts)), width)
    out_grad = jnp.stack(results, axis=0)[None]
    return (out_grad, down_sum.astype(jnp.bfloat16)[None, None])


def solution(mesh):
    return jax.shard_map(
        per_device,
        mesh=mesh,
        in_specs=(
            P("section", None, "expert", None),
            P("section", "expert", None),
            P(None, "expert", None),
            P("section", None, "expert", None),
            P("section", None, "expert", None),
            P("section", "expert", None, None),
            P("section", "expert", None, None),
            P("section", "expert", None, None),
        ),
        out_specs=(P("section", None, "expert", None), P("section", "expert", None, None)),
        check_vma=False,
    )
```

```python
import functools

import jax
import jax.numpy as jnp
from jax import lax
from jax.sharding import PartitionSpec as P

TOPK = 8
LANES = 128


def passed_along(value, axis, steps):
    count = lax.axis_size(axis)
    leading, last = (max(0, -steps), min(count, count - steps))
    return lax.ppermute(value, axis, [(source, source + steps) for source in range(leading, last)])


def slot_tables(expert_ids, probs, experts, slot_rows):
    ticks_here, tokens_here, choices_here = expert_ids.shape
    onehot = (expert_ids[..., None] == jnp.arange(experts, dtype=jnp.int32)).astype(jnp.int32)
    pairs = onehot.reshape(ticks_here, tokens_here * choices_here, experts)
    before = jnp.cumsum(pairs, axis=1) - pairs
    position = jnp.sum(before * pairs, axis=2).reshape(ticks_here, tokens_here, choices_here)
    target = expert_ids * slot_rows + position
    slots = jnp.arange(experts * slot_rows, dtype=jnp.int32)
    match = target[:, None, :, :] == slots[None, :, None, None]
    select = jnp.any(match, axis=3).astype(jnp.bfloat16)
    weight = jnp.sum(jnp.where(match, probs[:, None, :, :], 0.0), axis=(2, 3))
    return (select, weight)


def select_rows(select, source):
    return jnp.dot(select, source, preferred_element_type=jnp.float32)


def pack(rows, experts):
    return rows.reshape(experts, -1, LANES)


def unpack(block, width):
    return block.reshape(-1, width)


def exchange(block):
    return lax.all_to_all(block, "expert", split_axis=0, concat_axis=0, tiled=True)


def expert_backward(gate_pre, up_pre, sigma, grad_rows, gate_weight, up_weight, down_weight):
    contract = (((1,), (1,)), ((), ()))
    active = gate_pre * sigma
    hidden_grad = lax.dot_general(
        grad_rows, down_weight, contract, preferred_element_type=jnp.float32
    )
    gate_grad = (hidden_grad * up_pre * sigma * (1.0 + gate_pre * (1.0 - sigma))).astype(
        jnp.bfloat16
    )
    up_grad = (hidden_grad * active).astype(jnp.bfloat16)
    row_grad = lax.dot_general(gate_grad, gate_weight, contract, preferred_element_type=jnp.float32)
    row_grad = row_grad + lax.dot_general(
        up_grad, up_weight, contract, preferred_element_type=jnp.float32
    )
    return row_grad.astype(jnp.bfloat16)


def routed_rows(rows, experts, inner, slot_rows, width):
    outer = experts // inner
    expert = lax.axis_index("expert")
    here_z, here_x = expert // inner, expert % inner
    ticks_later = rows.shape[0]
    grid = rows.reshape(ticks_later, outer, inner, slot_rows, width)
    stage = []
    for step in range(inner):
        piece = lax.dynamic_index_in_dim(grid, (here_x + step) % inner, axis=2, keepdims=False)
        if step:
            pairs = [(j, j // inner * inner + (j % inner + step) % inner) for j in range(experts)]
            piece = lax.ppermute(piece, "expert", pairs)
        stage.append(piece)
    stage = jnp.stack(stage, axis=0)
    final = []
    for step in range(outer):
        piece = lax.dynamic_index_in_dim(stage, (here_z + step) % outer, axis=2, keepdims=False)
        if step:
            pairs = [(j, (j // inner + step) % outer * inner + j % inner) for j in range(experts)]
            piece = lax.ppermute(piece, "expert", pairs)
        final.append(piece)
    final = jnp.stack(final, axis=0)
    order_z = (here_z - jnp.arange(outer, dtype=jnp.int32)) % outer
    order_x = (here_x - jnp.arange(inner, dtype=jnp.int32)) % inner
    final = jnp.take(jnp.take(final, order_z, axis=0), order_x, axis=1)
    final = final.transpose(2, 0, 1, 3, 4)
    return final.reshape(ticks_later, experts * slot_rows, width)


def per_device(inner, acts, carried, loss_grad, expert_ids, probs, w_gate, w_up, w_down):
    experts = lax.axis_size("expert")
    ticks_here = acts.shape[1]
    tokens_here = acts.shape[2]
    width = acts.shape[3]
    slot_rows = min(tokens_here, 3 * tokens_here * TOPK // (2 * experts))
    gate_weight = w_gate[0, 0]
    up_weight = w_up[0, 0]
    down_weight = w_down[0, 0]
    is_last = lax.axis_index("section") == lax.axis_size("section") - 1
    select_all, weight_all = slot_tables(expert_ids[0], probs[0], experts, slot_rows)
    rows_contract = (((0,), (0,)), ((), ()))

    def grad_rows_of(moment, incoming):
        select, weight = select_all[moment], weight_all[moment]
        return (select_rows(select, incoming) * weight[:, None]).astype(jnp.bfloat16)

    incoming = jnp.where(is_last, loss_grad[0], carried[0])
    count = 2
    chooser = jnp.stack([select_all[0], select_all[0]], axis=0)
    sources = jnp.stack([acts[0, 0], incoming], axis=0)
    scale = jnp.stack([jnp.ones_like(weight_all[0]), weight_all[0]], axis=0)
    picked = lax.dot_general(
        chooser, sources, (((2,), (1,)), ((0,), (0,))), preferred_element_type=jnp.float32
    )
    picked = (picked * scale[:, :, None]).astype(jnp.bfloat16)
    send = picked.reshape(count, experts, -1, LANES).transpose(1, 0, 2, 3)
    received = exchange(send.reshape(experts, -1, LANES)).reshape(experts, count, -1, LANES)
    later = lax.dot_general(
        select_all[1:], acts[0, 1:], (((2,), (1,)), ((0,), (0,))),
        preferred_element_type=jnp.float32,
    ).astype(jnp.bfloat16)
    later_inputs = routed_rows(later, experts, inner, slot_rows, width)
    flat_grad = unpack(received[:, 1], width)

    results = []
    down_sum = jnp.zeros((down_weight.shape[0], width), jnp.float32)
    for moment in range(ticks_here):
        if moment == 0:
            received_input = unpack(received[:, 0], width)
        else:
            received_input = later_inputs[moment - 1]
        gate_pre = jnp.dot(received_input, gate_weight, preferred_element_type=jnp.float32)
        up_pre = jnp.dot(received_input, up_weight, preferred_element_type=jnp.float32)
        sigma = jax.nn.sigmoid(gate_pre)
        hidden = (gate_pre * sigma * up_pre).astype(jnp.bfloat16)
        row_grad = expert_backward(
            gate_pre, up_pre, sigma, flat_grad, gate_weight, up_weight, down_weight
        )
        returned = unpack(exchange(pack(row_grad, experts)), width)
        gathered = lax.dot_general(
            select_all[moment], returned, rows_contract, preferred_element_type=jnp.float32
        )
        result = (incoming.astype(jnp.float32) + gathered).astype(jnp.bfloat16)
        results.append(result)
        down_sum = down_sum + lax.dot_general(
            hidden, flat_grad, rows_contract, preferred_element_type=jnp.float32
        )
        if moment + 1 < ticks_here:
            arriving = passed_along(result, "section", -1)
            incoming = jnp.where(is_last, loss_grad[moment + 1], arriving)
            flat_grad = unpack(exchange(pack(grad_rows_of(moment + 1, incoming), experts)), width)
    out_grad = jnp.stack(results, axis=0)[None]
    return (out_grad, down_sum.astype(jnp.bfloat16)[None, None])


def inner_extent(mesh):
    try:
        row = list(mesh.devices.reshape(mesh.devices.shape[0], -1)[0])
        inner = len({device.coords[0] for device in row})
    except (AttributeError, IndexError, TypeError):
        inner = 1
    if inner < 1 or len(row) % inner:
        inner = 1
    return inner


def solution(mesh):
    return jax.shard_map(
        functools.partial(per_device, inner_extent(mesh)),
        mesh=mesh,
        in_specs=(
            P("section", None, "expert", None),
            P("section", "expert", None),
            P(None, "expert", None),
            P("section", None, "expert", None),
            P("section", None, "expert", None),
            P("section", "expert", None, None),
            P("section", "expert", None, None),
            P("section", "expert", None, None),
        ),
        out_specs=(P("section", None, "expert", None), P("section", "expert", None, None)),
        check_vma=False,
    )
```

```python
import jax
import jax.numpy as jnp
from jax import lax
from jax.sharding import PartitionSpec as P

TOPK = 8
LANES = 128


def passed_along(value, axis, steps):
    count = lax.axis_size(axis)
    leading, last = (max(0, -steps), min(count, count - steps))
    return lax.ppermute(value, axis, [(source, source + steps) for source in range(leading, last)])


def slot_tables(expert_ids, probs, experts, slot_rows):
    ticks_here, tokens_here, choices_here = expert_ids.shape
    onehot = (expert_ids[..., None] == jnp.arange(experts, dtype=jnp.int32)).astype(jnp.int32)
    pairs = onehot.reshape(ticks_here, tokens_here * choices_here, experts)
    before = jnp.cumsum(pairs, axis=1) - pairs
    position = jnp.sum(before * pairs, axis=2).reshape(ticks_here, tokens_here, choices_here)
    target = expert_ids * slot_rows + position
    slots = jnp.arange(experts * slot_rows, dtype=jnp.int32)
    match = target[:, None, :, :] == slots[None, :, None, None]
    select = jnp.any(match, axis=3).astype(jnp.bfloat16)
    weight = jnp.sum(jnp.where(match, probs[:, None, :, :], 0.0), axis=(2, 3))
    return (select, weight)


def select_rows(select, source):
    return jnp.dot(select, source, preferred_element_type=jnp.float32)


def pack(rows, experts):
    return rows.reshape(experts, -1, LANES)


def unpack(block, width):
    return block.reshape(-1, width)


def exchange(block):
    return lax.all_to_all(block, "expert", split_axis=0, concat_axis=0, tiled=True)


def expert_backward(gate_pre, up_pre, sigma, grad_rows, gate_weight, up_weight, down_weight):
    contract = (((1,), (1,)), ((), ()))
    active = gate_pre * sigma
    hidden_grad = lax.dot_general(
        grad_rows, down_weight, contract, preferred_element_type=jnp.float32
    )
    gate_grad = (hidden_grad * up_pre * sigma * (1.0 + gate_pre * (1.0 - sigma))).astype(
        jnp.bfloat16
    )
    up_grad = (hidden_grad * active).astype(jnp.bfloat16)
    row_grad = lax.dot_general(gate_grad, gate_weight, contract, preferred_element_type=jnp.float32)
    row_grad = row_grad + lax.dot_general(
        up_grad, up_weight, contract, preferred_element_type=jnp.float32
    )
    return row_grad.astype(jnp.bfloat16)


def per_device(acts, carried, loss_grad, expert_ids, probs, w_gate, w_up, w_down):
    experts = lax.axis_size("expert")
    ticks_here = acts.shape[1]
    tokens_here = acts.shape[2]
    width = acts.shape[3]
    slot_rows = min(tokens_here, 3 * tokens_here * TOPK // (2 * experts))
    gate_weight = w_gate[0, 0]
    up_weight = w_up[0, 0]
    down_weight = w_down[0, 0]
    is_last = lax.axis_index("section") == lax.axis_size("section") - 1
    select_all, weight_all = slot_tables(expert_ids[0], probs[0], experts, slot_rows)
    rows_contract = (((0,), (0,)), ((), ()))

    def grad_rows_of(moment, incoming):
        select, weight = select_all[moment], weight_all[moment]
        return (select_rows(select, incoming) * weight[:, None]).astype(jnp.bfloat16)

    incoming = jnp.where(is_last, loss_grad[0], carried[0])
    count = ticks_here + 1
    tokens_here = acts.shape[2]
    chooser = jnp.concatenate([select_all, select_all[:1]], axis=0)
    chooser = chooser.reshape(count, experts, slot_rows, tokens_here).transpose(1, 0, 2, 3)
    blocks = jnp.eye(count, dtype=jnp.bfloat16)[None, :, None, :, None]
    chooser = (chooser[:, :, :, None, :] * blocks).reshape(experts, count * slot_rows, -1)
    scale = jnp.concatenate(
        [jnp.ones((ticks_here, select_all.shape[1]), jnp.float32), weight_all[:1]], axis=0
    )
    scale = scale.reshape(count, experts, slot_rows).transpose(1, 0, 2).reshape(experts, -1)
    aligned = -(-count * slot_rows // 16) * 16
    spare = aligned - count * slot_rows
    chooser = jnp.pad(chooser, ((0, 0), (0, spare), (0, 0)))
    scale = jnp.pad(scale, ((0, 0), (0, spare)))
    sources = jnp.concatenate([acts[0], incoming[None]], axis=0).reshape(-1, width)
    picked = lax.dot_general(
        chooser, sources, (((2,), (0,)), ((), ())), preferred_element_type=jnp.float32
    )
    send = (picked * scale[:, :, None]).astype(jnp.bfloat16)
    received = exchange(send)[:, : count * slot_rows].reshape(experts, count, slot_rows, width)
    flat_grad = received[:, ticks_here].reshape(-1, width)

    results = []
    down_sum = jnp.zeros((down_weight.shape[0], width), jnp.float32)
    for moment in range(ticks_here):
        received_input = received[:, moment].reshape(-1, width)
        gate_pre = jnp.dot(received_input, gate_weight, preferred_element_type=jnp.float32)
        up_pre = jnp.dot(received_input, up_weight, preferred_element_type=jnp.float32)
        sigma = jax.nn.sigmoid(gate_pre)
        hidden = (gate_pre * sigma * up_pre).astype(jnp.bfloat16)
        row_grad = expert_backward(
            gate_pre, up_pre, sigma, flat_grad, gate_weight, up_weight, down_weight
        )
        returned = unpack(exchange(pack(row_grad, experts)), width)
        gathered = lax.dot_general(
            select_all[moment], returned, rows_contract, preferred_element_type=jnp.float32
        )
        result = (incoming.astype(jnp.float32) + gathered).astype(jnp.bfloat16)
        results.append(result)
        down_sum = down_sum + lax.dot_general(
            hidden, flat_grad, rows_contract, preferred_element_type=jnp.float32
        )
        if moment + 1 < ticks_here:
            arriving = passed_along(result, "section", -1)
            incoming = jnp.where(is_last, loss_grad[moment + 1], arriving)
            flat_grad = unpack(exchange(pack(grad_rows_of(moment + 1, incoming), experts)), width)
    out_grad = jnp.stack(results, axis=0)[None]
    return (out_grad, down_sum.astype(jnp.bfloat16)[None, None])


def solution(mesh):
    return jax.shard_map(
        per_device,
        mesh=mesh,
        in_specs=(
            P("section", None, "expert", None),
            P("section", "expert", None),
            P(None, "expert", None),
            P("section", None, "expert", None),
            P("section", None, "expert", None),
            P("section", "expert", None, None),
            P("section", "expert", None, None),
            P("section", "expert", None, None),
        ),
        out_specs=(P("section", None, "expert", None), P("section", "expert", None, None)),
        check_vma=False,
    )
```

```python
import jax
import jax.numpy as jnp
from jax import lax
from jax.sharding import PartitionSpec as P

TOPK = 8
LANES = 128


def passed_along(value, axis, steps):
    count = lax.axis_size(axis)
    leading, last = (max(0, -steps), min(count, count - steps))
    return lax.ppermute(value, axis, [(source, source + steps) for source in range(leading, last)])


def slot_tables(expert_ids, probs, experts, slot_rows):
    ticks_here, tokens_here, choices_here = expert_ids.shape
    onehot = (expert_ids[..., None] == jnp.arange(experts, dtype=jnp.int32)).astype(jnp.int32)
    pairs = onehot.reshape(ticks_here, tokens_here * choices_here, experts)
    before = jnp.cumsum(pairs, axis=1) - pairs
    position = jnp.sum(before * pairs, axis=2).reshape(ticks_here, tokens_here, choices_here)
    target = expert_ids * slot_rows + position
    slots = jnp.arange(experts * slot_rows, dtype=jnp.int32)
    match = target[:, None, :, :] == slots[None, :, None, None]
    select = jnp.any(match, axis=3).astype(jnp.bfloat16)
    weight = jnp.sum(jnp.where(match, probs[:, None, :, :], 0.0), axis=(2, 3))
    return (select, weight)


def select_rows(select, source):
    return jnp.dot(select, source, preferred_element_type=jnp.float32)


def pack(rows, experts):
    return rows.reshape(experts, -1, LANES)


def unpack(block, width):
    return block.reshape(-1, width)


def exchange(block):
    return lax.all_to_all(block, "expert", split_axis=0, concat_axis=0, tiled=True)


def expert_backward(gate_pre, up_pre, sigma, grad_rows, both_weight, down_weight):
    contract = (((1,), (1,)), ((), ()))
    active = gate_pre * sigma
    hidden_grad = lax.dot_general(
        grad_rows, down_weight, contract, preferred_element_type=jnp.float32
    )
    gate_grad = (hidden_grad * up_pre * sigma * (1.0 + gate_pre * (1.0 - sigma))).astype(
        jnp.bfloat16
    )
    up_grad = (hidden_grad * active).astype(jnp.bfloat16)
    both_grad = jnp.concatenate([gate_grad, up_grad], axis=1)
    row_grad = lax.dot_general(both_grad, both_weight, contract, preferred_element_type=jnp.float32)
    return row_grad.astype(jnp.bfloat16)


def per_device(acts, carried, loss_grad, expert_ids, probs, w_gate, w_up, w_down):
    experts = lax.axis_size("expert")
    ticks_here = acts.shape[1]
    tokens_here = acts.shape[2]
    width = acts.shape[3]
    slot_rows = min(tokens_here, 3 * tokens_here * TOPK // (2 * experts))
    gate_weight = w_gate[0, 0]
    up_weight = w_up[0, 0]
    down_weight = w_down[0, 0]
    both_weight = jnp.concatenate([gate_weight, up_weight], axis=1)
    hidden_units = gate_weight.shape[1]
    is_last = lax.axis_index("section") == lax.axis_size("section") - 1
    select_all, weight_all = slot_tables(expert_ids[0], probs[0], experts, slot_rows)
    rows_contract = (((0,), (0,)), ((), ()))

    def grad_rows_of(moment, incoming):
        select, weight = select_all[moment], weight_all[moment]
        return (select_rows(select, incoming) * weight[:, None]).astype(jnp.bfloat16)

    incoming = jnp.where(is_last, loss_grad[0], carried[0])
    count = ticks_here + 1
    chooser = jnp.concatenate([select_all, select_all[:1]], axis=0)
    sources = jnp.concatenate([acts[0], incoming[None]], axis=0)
    scale = jnp.concatenate(
        [jnp.ones((ticks_here, select_all.shape[1]), jnp.float32), weight_all[:1]], axis=0
    )
    picked = lax.dot_general(
        chooser, sources, (((2,), (1,)), ((0,), (0,))), preferred_element_type=jnp.float32
    )
    picked = (picked * scale[:, :, None]).astype(jnp.bfloat16)
    send = picked.reshape(count, experts, -1, LANES).transpose(1, 0, 2, 3)
    received = exchange(send.reshape(experts, -1, LANES)).reshape(experts, count, -1, LANES)
    flat_grad = unpack(received[:, ticks_here], width)

    results = []
    down_sum = jnp.zeros((down_weight.shape[0], width), jnp.float32)
    for moment in range(ticks_here):
        received_input = unpack(received[:, moment], width)
        both_pre = jnp.dot(received_input, both_weight, preferred_element_type=jnp.float32)
        gate_pre, up_pre = both_pre[:, :hidden_units], both_pre[:, hidden_units:]
        sigma = jax.nn.sigmoid(gate_pre)
        hidden = (gate_pre * sigma * up_pre).astype(jnp.bfloat16)
        row_grad = expert_backward(
            gate_pre, up_pre, sigma, flat_grad, both_weight, down_weight
        )
        returned = unpack(exchange(pack(row_grad, experts)), width)
        gathered = lax.dot_general(
            select_all[moment], returned, rows_contract, preferred_element_type=jnp.float32
        )
        result = (incoming.astype(jnp.float32) + gathered).astype(jnp.bfloat16)
        results.append(result)
        down_sum = down_sum + lax.dot_general(
            hidden, flat_grad, rows_contract, preferred_element_type=jnp.float32
        )
        if moment + 1 < ticks_here:
            arriving = passed_along(result, "section", -1)
            incoming = jnp.where(is_last, loss_grad[moment + 1], arriving)
            flat_grad = unpack(exchange(pack(grad_rows_of(moment + 1, incoming), experts)), width)
    out_grad = jnp.stack(results, axis=0)[None]
    return (out_grad, down_sum.astype(jnp.bfloat16)[None, None])


def solution(mesh):
    return jax.shard_map(
        per_device,
        mesh=mesh,
        in_specs=(
            P("section", None, "expert", None),
            P("section", "expert", None),
            P(None, "expert", None),
            P("section", None, "expert", None),
            P("section", None, "expert", None),
            P("section", "expert", None, None),
            P("section", "expert", None, None),
            P("section", "expert", None, None),
        ),
        out_specs=(P("section", None, "expert", None), P("section", "expert", None, None)),
        check_vma=False,
    )
```

```python
import jax
import jax.numpy as jnp
from jax import lax
from jax.sharding import PartitionSpec as P


TOPK = 8
LANES = 128


def passed_along(value, axis, steps):
    count = lax.axis_size(axis)
    leading, last = (max(0, -steps), min(count, count - steps))
    return lax.ppermute(value, axis, [(source, source + steps) for source in range(leading, last)])


def slot_tables(expert_ids, probs, experts, slot_rows):
    ticks_here, tokens_here, choices_here = expert_ids.shape
    onehot = (expert_ids[..., None] == jnp.arange(experts, dtype=jnp.int32)).astype(jnp.int32)
    pairs = onehot.reshape(ticks_here, tokens_here * choices_here, experts)
    before = jnp.cumsum(pairs, axis=1) - pairs
    position = jnp.sum(before * pairs, axis=2).reshape(ticks_here, tokens_here, choices_here)
    target = expert_ids * slot_rows + position
    slots = jnp.arange(experts * slot_rows, dtype=jnp.int32)
    match = target[:, None, :, :] == slots[None, :, None, None]
    select = jnp.any(match, axis=3).astype(jnp.bfloat16)
    weight = jnp.sum(jnp.where(match, probs[:, None, :, :], 0.0), axis=(2, 3))
    return (select, weight)


def select_rows(select, source):
    return jnp.dot(select, source, preferred_element_type=jnp.float32)


def pack(rows, experts):
    return rows.reshape(experts, -1, LANES)


def unpack(block, width):
    return block.reshape(-1, width)


def exchange(block):
    return lax.all_to_all(block, "expert", split_axis=0, concat_axis=0, tiled=True)


def expert_backward(gate_pre, up_pre, sigma, grad_rows, both_weight, down_weight):
    contract = (((1,), (1,)), ((), ()))
    active = gate_pre * sigma
    hidden_grad = lax.dot_general(
        grad_rows, down_weight, contract, preferred_element_type=jnp.float32
    )
    gate_grad = (hidden_grad * up_pre * sigma * (1.0 + gate_pre * (1.0 - sigma))).astype(
        jnp.bfloat16
    )
    up_grad = (hidden_grad * active).astype(jnp.bfloat16)
    both_grad = jnp.concatenate([gate_grad, up_grad], axis=1)
    row_grad = lax.dot_general(both_grad, both_weight, contract, preferred_element_type=jnp.float32)
    return row_grad.astype(jnp.bfloat16)


def per_device(acts, carried, loss_grad, expert_ids, probs, w_gate, w_up, w_down):
    experts = lax.axis_size("expert")
    ticks_here = acts.shape[1]
    tokens_here = acts.shape[2]
    width = acts.shape[3]
    slot_rows = min(tokens_here, 3 * tokens_here * TOPK // (2 * experts))
    gate_weight = w_gate[0, 0]
    up_weight = w_up[0, 0]
    down_weight = w_down[0, 0]
    both_weight = jnp.concatenate([gate_weight, up_weight], axis=1)
    hidden_units = gate_weight.shape[1]
    is_last = lax.axis_index("section") == lax.axis_size("section") - 1
    select_all, weight_all = slot_tables(expert_ids[0], probs[0], experts, slot_rows)
    rows_contract = (((0,), (0,)), ((), ()))

    def grad_rows_of(moment, incoming):
        select, weight = select_all[moment], weight_all[moment]
        return (select_rows(select, incoming) * weight[:, None]).astype(jnp.bfloat16)

    incoming = jnp.where(is_last, loss_grad[0], carried[0])
    count = ticks_here + 1
    chooser = jnp.concatenate([select_all, select_all[:1]], axis=0)
    sources = jnp.concatenate([acts[0], incoming[None]], axis=0)
    scale = jnp.concatenate(
        [jnp.ones((ticks_here, select_all.shape[1]), jnp.float32), weight_all[:1]], axis=0
    )
    picked = lax.dot_general(
        chooser, sources, (((2,), (1,)), ((0,), (0,))), preferred_element_type=jnp.float32
    )
    picked = (picked * scale[:, :, None]).astype(jnp.bfloat16)
    send = picked.reshape(count, experts, -1, LANES).transpose(1, 0, 2, 3)
    received = exchange(send.reshape(experts, -1, LANES)).reshape(experts, count, -1, LANES)
    flat_grad = unpack(received[:, ticks_here], width)

    results = []
    down_sum = jnp.zeros((down_weight.shape[0], width), jnp.float32)
    for moment in range(ticks_here):
        received_input = unpack(received[:, moment], width)
        both_pre = jnp.dot(received_input, both_weight, preferred_element_type=jnp.float32)
        gate_pre, up_pre = both_pre[:, :hidden_units], both_pre[:, hidden_units:]
        sigma = jax.nn.sigmoid(gate_pre)
        hidden = (gate_pre * sigma * up_pre).astype(jnp.bfloat16)
        row_grad = expert_backward(
            gate_pre, up_pre, sigma, flat_grad, both_weight, down_weight
        )
        returned = unpack(exchange(pack(row_grad, experts)), width)
        gathered = lax.dot_general(
            select_all[moment], returned, rows_contract, preferred_element_type=jnp.float32
        )
        result = (incoming.astype(jnp.float32) + gathered).astype(jnp.bfloat16)
        results.append(result)
        term = lax.dot_general(hidden, flat_grad, rows_contract, preferred_element_type=jnp.float32)
        down_sum = down_sum + term
        if moment + 1 < ticks_here:
            arriving = passed_along(result, "section", -1)
            incoming = jnp.where(is_last, loss_grad[moment + 1], arriving)
            flat_grad = unpack(exchange(pack(grad_rows_of(moment + 1, incoming), experts)), width)
    out_grad = jnp.stack(results, axis=0)[None]
    return (out_grad, down_sum.astype(jnp.bfloat16)[None, None])


def solution(mesh):
    return jax.shard_map(
        per_device,
        mesh=mesh,
        in_specs=(
            P("section", None, "expert", None),
            P("section", "expert", None),
            P(None, "expert", None),
            P("section", None, "expert", None),
            P("section", None, "expert", None),
            P("section", "expert", None, None),
            P("section", "expert", None, None),
            P("section", "expert", None, None),
        ),
        out_specs=(P("section", None, "expert", None), P("section", "expert", None, None)),
        check_vma=False,
    )
```

```python
import jax
import jax.numpy as jnp
from jax import lax
from jax.sharding import PartitionSpec as P

TOPK = 8
LANES = 128


def passed_along(value, axis, steps):
    count = lax.axis_size(axis)
    leading, last = (max(0, -steps), min(count, count - steps))
    return lax.ppermute(value, axis, [(source, source + steps) for source in range(leading, last)])


def slot_tables(expert_ids, probs, experts, slot_rows):
    ticks_here, tokens_here, choices_here = expert_ids.shape
    onehot = (expert_ids[..., None] == jnp.arange(experts, dtype=jnp.int32)).astype(jnp.int32)
    pairs = onehot.reshape(ticks_here, tokens_here * choices_here, experts)
    count = tokens_here * choices_here
    earlier = (
        jnp.arange(count, dtype=jnp.int32)[None, :] < jnp.arange(count, dtype=jnp.int32)[:, None]
    ).astype(jnp.bfloat16)
    before = jnp.einsum(
        "ij,tje->tie", earlier, pairs.astype(jnp.bfloat16), preferred_element_type=jnp.float32
    ).astype(jnp.int32)
    position = jnp.sum(before * pairs, axis=2).reshape(ticks_here, tokens_here, choices_here)
    target = expert_ids * slot_rows + position
    slots = jnp.arange(experts * slot_rows, dtype=jnp.int32)
    match = target[:, None, :, :] == slots[None, :, None, None]
    select = jnp.any(match, axis=3).astype(jnp.bfloat16)
    weight = jnp.sum(jnp.where(match, probs[:, None, :, :], 0.0), axis=(2, 3))
    return (select, weight)


def select_rows(select, source):
    return jnp.dot(select, source, preferred_element_type=jnp.float32)


def pack(rows, experts):
    return rows.reshape(experts, -1, LANES)


def unpack(block, width):
    return block.reshape(-1, width)


def exchange(block):
    return lax.all_to_all(block, "expert", split_axis=0, concat_axis=0, tiled=True)


def expert_backward(gate_pre, up_pre, sigma, grad_rows, both_weight, down_weight):
    contract = (((1,), (1,)), ((), ()))
    active = gate_pre * sigma
    hidden_grad = lax.dot_general(
        grad_rows, down_weight, contract, preferred_element_type=jnp.float32
    )
    gate_grad = (hidden_grad * up_pre * sigma * (1.0 + gate_pre * (1.0 - sigma))).astype(
        jnp.bfloat16
    )
    up_grad = (hidden_grad * active).astype(jnp.bfloat16)
    both_grad = jnp.concatenate([gate_grad, up_grad], axis=1)
    row_grad = lax.dot_general(both_grad, both_weight, contract, preferred_element_type=jnp.float32)
    return row_grad.astype(jnp.bfloat16)


def per_device(acts, carried, loss_grad, expert_ids, probs, w_gate, w_up, w_down):
    experts = lax.axis_size("expert")
    ticks_here = acts.shape[1]
    tokens_here = acts.shape[2]
    width = acts.shape[3]
    slot_rows = min(tokens_here, 3 * tokens_here * TOPK // (2 * experts))
    gate_weight = w_gate[0, 0]
    up_weight = w_up[0, 0]
    down_weight = w_down[0, 0]
    both_weight = jnp.concatenate([gate_weight, up_weight], axis=1)
    hidden_units = gate_weight.shape[1]
    is_last = lax.axis_index("section") == lax.axis_size("section") - 1
    select_all, weight_all = slot_tables(expert_ids[0], probs[0], experts, slot_rows)
    rows_contract = (((0,), (0,)), ((), ()))

    def grad_rows_of(moment, incoming):
        select, weight = select_all[moment], weight_all[moment]
        return (select_rows(select, incoming) * weight[:, None]).astype(jnp.bfloat16)

    incoming = jnp.where(is_last, loss_grad[0], carried[0])
    count = ticks_here + 1
    chooser = jnp.concatenate([select_all, select_all[:1]], axis=0)
    sources = jnp.concatenate([acts[0], incoming[None]], axis=0)
    scale = jnp.concatenate(
        [jnp.ones((ticks_here, select_all.shape[1]), jnp.float32), weight_all[:1]], axis=0
    )
    picked = lax.dot_general(
        chooser, sources, (((2,), (1,)), ((0,), (0,))), preferred_element_type=jnp.float32
    )
    picked = (picked * scale[:, :, None]).astype(jnp.bfloat16)
    send = picked.reshape(count, experts, -1, LANES).transpose(1, 0, 2, 3)
    received = exchange(send.reshape(experts, -1, LANES)).reshape(experts, count, -1, LANES)
    flat_grad = unpack(received[:, ticks_here], width)

    results = []
    down_sum = jnp.zeros((down_weight.shape[0], width), jnp.float32)
    for moment in range(ticks_here):
        received_input = unpack(received[:, moment], width)
        both_pre = jnp.dot(received_input, both_weight, preferred_element_type=jnp.float32)
        gate_pre, up_pre = both_pre[:, :hidden_units], both_pre[:, hidden_units:]
        sigma = jax.nn.sigmoid(gate_pre)
        hidden = (gate_pre * sigma * up_pre).astype(jnp.bfloat16)
        row_grad = expert_backward(
            gate_pre, up_pre, sigma, flat_grad, both_weight, down_weight
        )
        returned = unpack(exchange(pack(row_grad, experts)), width)
        gathered = lax.dot_general(
            select_all[moment], returned, rows_contract, preferred_element_type=jnp.float32
        )
        result = (incoming.astype(jnp.float32) + gathered).astype(jnp.bfloat16)
        results.append(result)
        down_sum = down_sum + lax.dot_general(
            hidden, flat_grad, rows_contract, preferred_element_type=jnp.float32
        )
        if moment + 1 < ticks_here:
            arriving = passed_along(result, "section", -1)
            incoming = jnp.where(is_last, loss_grad[moment + 1], arriving)
            flat_grad = unpack(exchange(pack(grad_rows_of(moment + 1, incoming), experts)), width)
    out_grad = jnp.stack(results, axis=0)[None]
    return (out_grad, down_sum.astype(jnp.bfloat16)[None, None])


def solution(mesh):
    return jax.shard_map(
        per_device,
        mesh=mesh,
        in_specs=(
            P("section", None, "expert", None),
            P("section", "expert", None),
            P(None, "expert", None),
            P("section", None, "expert", None),
            P("section", None, "expert", None),
            P("section", "expert", None, None),
            P("section", "expert", None, None),
            P("section", "expert", None, None),
        ),
        out_specs=(P("section", None, "expert", None), P("section", "expert", None, None)),
        check_vma=False,
    )
```

```python
import jax
import jax.numpy as jnp
from jax import lax
from jax.sharding import PartitionSpec as P

TOPK = 8
LANES = 128


def passed_along(value, axis, steps):
    count = lax.axis_size(axis)
    leading, last = (max(0, -steps), min(count, count - steps))
    return lax.ppermute(value, axis, [(source, source + steps) for source in range(leading, last)])


def slot_tables(expert_ids, probs, experts, slot_rows):
    ticks_here, tokens_here, choices_here = expert_ids.shape
    onehot = (expert_ids[..., None] == jnp.arange(experts, dtype=jnp.int32)).astype(jnp.int32)
    pairs = onehot.reshape(ticks_here, tokens_here * choices_here, experts)
    count = tokens_here * choices_here
    earlier = (
        jnp.arange(count, dtype=jnp.int32)[None, :] < jnp.arange(count, dtype=jnp.int32)[:, None]
    ).astype(jnp.bfloat16)
    before = jnp.einsum(
        "ij,tje->tie", earlier, pairs.astype(jnp.bfloat16), preferred_element_type=jnp.float32
    ).astype(jnp.int32)
    position = jnp.sum(before * pairs, axis=2).reshape(ticks_here, tokens_here, choices_here)
    target = expert_ids * slot_rows + position
    slots = jnp.arange(experts * slot_rows, dtype=jnp.int32)
    match = target[:, None, :, :] == slots[None, :, None, None]
    select = jnp.any(match, axis=3).astype(jnp.bfloat16)
    weight = jnp.sum(jnp.where(match, probs[:, None, :, :], 0.0), axis=(2, 3))
    return (select, weight)


def select_rows(select, source):
    return jnp.dot(select, source, preferred_element_type=jnp.float32)


def pack(rows, experts):
    return rows.reshape(experts, -1, LANES)


def unpack(block, width):
    return block.reshape(-1, width)


def exchange(block):
    return lax.all_to_all(block, "expert", split_axis=0, concat_axis=0, tiled=True)


def expert_backward(gate_factor, active, grad_rows, both_weight, down_weight):
    contract = (((1,), (1,)), ((), ()))
    hidden_grad = lax.dot_general(
        grad_rows, down_weight, contract, preferred_element_type=jnp.float32
    )
    gate_grad = (hidden_grad * gate_factor).astype(jnp.bfloat16)
    up_grad = (hidden_grad * active).astype(jnp.bfloat16)
    both_grad = jnp.concatenate([gate_grad, up_grad], axis=1)
    row_grad = lax.dot_general(both_grad, both_weight, contract, preferred_element_type=jnp.float32)
    return row_grad.astype(jnp.bfloat16)


def per_device(acts, carried, loss_grad, expert_ids, probs, w_gate, w_up, w_down):
    experts = lax.axis_size("expert")
    ticks_here = acts.shape[1]
    tokens_here = acts.shape[2]
    width = acts.shape[3]
    slot_rows = min(tokens_here, 3 * tokens_here * TOPK // (2 * experts))
    gate_weight = w_gate[0, 0]
    up_weight = w_up[0, 0]
    down_weight = w_down[0, 0]
    both_weight = jnp.concatenate([gate_weight, up_weight], axis=1)
    hidden_units = gate_weight.shape[1]
    is_last = lax.axis_index("section") == lax.axis_size("section") - 1
    select_all, weight_all = slot_tables(expert_ids[0], probs[0], experts, slot_rows)
    rows_contract = (((0,), (0,)), ((), ()))

    def grad_rows_of(moment, incoming):
        select, weight = select_all[moment], weight_all[moment]
        return (select_rows(select, incoming) * weight[:, None]).astype(jnp.bfloat16)

    incoming = jnp.where(is_last, loss_grad[0], carried[0])
    count = ticks_here + 1
    chooser = jnp.concatenate([select_all, select_all[:1]], axis=0)
    sources = jnp.concatenate([acts[0], incoming[None]], axis=0)
    scale = jnp.concatenate(
        [jnp.ones((ticks_here, select_all.shape[1]), jnp.float32), weight_all[:1]], axis=0
    )
    picked = lax.dot_general(
        chooser, sources, (((2,), (1,)), ((0,), (0,))), preferred_element_type=jnp.float32
    )
    picked = (picked * scale[:, :, None]).astype(jnp.bfloat16)
    send = picked.reshape(count, experts, -1, LANES).transpose(1, 0, 2, 3)
    received = exchange(send.reshape(experts, -1, LANES)).reshape(experts, count, -1, LANES)
    flat_grad = unpack(received[:, ticks_here], width)

    results = []
    down_sum = jnp.zeros((down_weight.shape[0], width), jnp.float32)
    for moment in range(ticks_here):
        received_input = unpack(received[:, moment], width)
        both_pre = jnp.dot(received_input, both_weight, preferred_element_type=jnp.float32)
        gate_pre, up_pre = both_pre[:, :hidden_units], both_pre[:, hidden_units:]
        sigma = jax.nn.sigmoid(gate_pre)
        active = gate_pre * sigma
        hidden = (active * up_pre).astype(jnp.bfloat16)
        gate_factor = up_pre * sigma * (1.0 + gate_pre * (1.0 - sigma))
        gate_factor, active = lax.optimization_barrier((gate_factor, active))
        row_grad = expert_backward(gate_factor, active, flat_grad, both_weight, down_weight)
        returned = unpack(exchange(pack(row_grad, experts)), width)
        gathered = lax.dot_general(
            select_all[moment], returned, rows_contract, preferred_element_type=jnp.float32
        )
        result = (incoming.astype(jnp.float32) + gathered).astype(jnp.bfloat16)
        results.append(result)
        down_sum = down_sum + lax.dot_general(
            hidden, flat_grad, rows_contract, preferred_element_type=jnp.float32
        )
        if moment + 1 < ticks_here:
            arriving = passed_along(result, "section", -1)
            incoming = jnp.where(is_last, loss_grad[moment + 1], arriving)
            flat_grad = unpack(exchange(pack(grad_rows_of(moment + 1, incoming), experts)), width)
    out_grad = jnp.stack(results, axis=0)[None]
    return (out_grad, down_sum.astype(jnp.bfloat16)[None, None])


def solution(mesh):
    return jax.shard_map(
        per_device,
        mesh=mesh,
        in_specs=(
            P("section", None, "expert", None),
            P("section", "expert", None),
            P(None, "expert", None),
            P("section", None, "expert", None),
            P("section", None, "expert", None),
            P("section", "expert", None, None),
            P("section", "expert", None, None),
            P("section", "expert", None, None),
        ),
        out_specs=(P("section", None, "expert", None), P("section", "expert", None, None)),
        check_vma=False,
    )
```

```python
import jax
import jax.numpy as jnp
from jax import lax
from jax.sharding import PartitionSpec as P

TOPK = 8
LANES = 128


def passed_along(value, axis, steps):
    count = lax.axis_size(axis)
    leading, last = (max(0, -steps), min(count, count - steps))
    return lax.ppermute(value, axis, [(source, source + steps) for source in range(leading, last)])


def slot_tables(expert_ids, probs, experts, slot_rows):
    ticks_here, tokens_here, choices_here = expert_ids.shape
    onehot = (expert_ids[..., None] == jnp.arange(experts, dtype=jnp.int32)).astype(jnp.int32)
    pairs = onehot.reshape(ticks_here, tokens_here * choices_here, experts)
    count = tokens_here * choices_here
    earlier = (
        jnp.arange(count, dtype=jnp.int32)[None, :] < jnp.arange(count, dtype=jnp.int32)[:, None]
    ).astype(jnp.bfloat16)
    before = jnp.einsum(
        "ij,tje->tie", earlier, pairs.astype(jnp.bfloat16), preferred_element_type=jnp.float32
    ).astype(jnp.int32)
    position = jnp.sum(before * pairs, axis=2).reshape(ticks_here, tokens_here, choices_here)
    target = expert_ids * slot_rows + position
    slots = jnp.arange(experts * slot_rows, dtype=jnp.int32)
    match = target[:, None, :, :] == slots[None, :, None, None]
    select = jnp.any(match, axis=3).astype(jnp.bfloat16)
    weight = jnp.sum(jnp.where(match, probs[:, None, :, :], 0.0), axis=(2, 3))
    return (select, weight)


def select_rows(select, source):
    return jnp.dot(select, source, preferred_element_type=jnp.float32)


def pack(rows, experts):
    return rows.reshape(experts, -1, LANES)


def unpack(block, width):
    return block.reshape(-1, width)


def exchange(block):
    return lax.all_to_all(block, "expert", split_axis=0, concat_axis=0, tiled=True)


def expert_backward(gate_factor, active, grad_rows, both_weight, down_weight):
    contract = (((1,), (1,)), ((), ()))
    hidden_grad = jnp.dot(grad_rows, down_weight, preferred_element_type=jnp.float32)
    gate_grad = (hidden_grad * gate_factor).astype(jnp.bfloat16)
    up_grad = (hidden_grad * active).astype(jnp.bfloat16)
    both_grad = jnp.concatenate([gate_grad, up_grad], axis=1)
    row_grad = lax.dot_general(both_grad, both_weight, contract, preferred_element_type=jnp.float32)
    return row_grad.astype(jnp.bfloat16)


def per_device(acts, carried, loss_grad, expert_ids, probs, w_gate, w_up, w_down):
    experts = lax.axis_size("expert")
    ticks_here = acts.shape[1]
    tokens_here = acts.shape[2]
    width = acts.shape[3]
    slot_rows = min(tokens_here, 3 * tokens_here * TOPK // (2 * experts))
    gate_weight = w_gate[0, 0]
    up_weight = w_up[0, 0]
    down_weight = w_down[0, 0]
    down_across = lax.optimization_barrier(down_weight.T)
    both_weight = jnp.concatenate([gate_weight, up_weight], axis=1)
    hidden_units = gate_weight.shape[1]
    is_last = lax.axis_index("section") == lax.axis_size("section") - 1
    select_all, weight_all = slot_tables(expert_ids[0], probs[0], experts, slot_rows)
    rows_contract = (((0,), (0,)), ((), ()))

    def grad_rows_of(moment, incoming):
        select, weight = select_all[moment], weight_all[moment]
        return (select_rows(select, incoming) * weight[:, None]).astype(jnp.bfloat16)

    incoming = jnp.where(is_last, loss_grad[0], carried[0])
    count = ticks_here + 1
    chooser = jnp.concatenate([select_all, select_all[:1]], axis=0)
    sources = jnp.concatenate([acts[0], incoming[None]], axis=0)
    scale = jnp.concatenate(
        [jnp.ones((ticks_here, select_all.shape[1]), jnp.float32), weight_all[:1]], axis=0
    )
    picked = lax.dot_general(
        chooser, sources, (((2,), (1,)), ((0,), (0,))), preferred_element_type=jnp.float32
    )
    picked = (picked * scale[:, :, None]).astype(jnp.bfloat16)
    send = picked.reshape(count, experts, -1, LANES).transpose(1, 0, 2, 3)
    received = exchange(send.reshape(experts, -1, LANES)).reshape(experts, count, -1, LANES)
    flat_grad = unpack(received[:, ticks_here], width)

    results = []
    down_sum = jnp.zeros((down_weight.shape[0], width), jnp.float32)
    for moment in range(ticks_here):
        received_input = unpack(received[:, moment], width)
        both_pre = jnp.dot(received_input, both_weight, preferred_element_type=jnp.float32)
        gate_pre, up_pre = both_pre[:, :hidden_units], both_pre[:, hidden_units:]
        sigma = jax.nn.sigmoid(gate_pre)
        active = gate_pre * sigma
        hidden = (active * up_pre).astype(jnp.bfloat16)
        gate_factor = up_pre * sigma * (1.0 + gate_pre * (1.0 - sigma))
        gate_factor, active = lax.optimization_barrier((gate_factor, active))
        row_grad = expert_backward(gate_factor, active, flat_grad, both_weight, down_across)
        returned = unpack(exchange(pack(row_grad, experts)), width)
        gathered = lax.dot_general(
            select_all[moment], returned, rows_contract, preferred_element_type=jnp.float32
        )
        result = (incoming.astype(jnp.float32) + gathered).astype(jnp.bfloat16)
        results.append(result)
        down_sum = down_sum + lax.dot_general(
            hidden, flat_grad, rows_contract, preferred_element_type=jnp.float32
        )
        if moment + 1 < ticks_here:
            arriving = passed_along(result, "section", -1)
            incoming = jnp.where(is_last, loss_grad[moment + 1], arriving)
            flat_grad = unpack(exchange(pack(grad_rows_of(moment + 1, incoming), experts)), width)
    out_grad = jnp.stack(results, axis=0)[None]
    return (out_grad, down_sum.astype(jnp.bfloat16)[None, None])


def solution(mesh):
    return jax.shard_map(
        per_device,
        mesh=mesh,
        in_specs=(
            P("section", None, "expert", None),
            P("section", "expert", None),
            P(None, "expert", None),
            P("section", None, "expert", None),
            P("section", None, "expert", None),
            P("section", "expert", None, None),
            P("section", "expert", None, None),
            P("section", "expert", None, None),
        ),
        out_specs=(P("section", None, "expert", None), P("section", "expert", None, None)),
        check_vma=False,
    )
```
